128 devices in a mesh: band: 4 (over x), pair: 32 (over z, y, core).
Axes of the slice: x: 4, y: 4, z: 4, core: 2. Of those that a mesh axis runs over, the one named last changes fastest.
Arguments:
- traces: float32 [16, 8192, 1024], P('band', 'pair'), may hold values from -300 to 300
- pair_list: int32 [256, 2], replicated, may hold values from 0 to 63, as said below
- pair_owner: int32 [256], replicated, may hold values from 0 to 63, as said below
Outputs:
- cross_spectra: bfloat16 [64, 2, 128, 128, 512], P('pair', None, None, None, 'band')
The draws below stay inside these ranges and needn't reach their ends.
Inputs may be any that keep to these rules, and one draw needn't show every extreme that they name: `pair_list`: each row (i, j) has 8 <= j - i <= 24; index p of pair holds blocks p * 64 / 32 up to (p + 1) * 64 / 32 - 1, and the 16 blocks named by the rows of one owner (pair_owner // 2) all lie on different indices of pair. `pair_owner`: every slot is named by exactly 4 rows.
All inputs are finite; a program needn't handle non-finite values.
Results may differ from the reference program's by a relative error of at most 0.0057.
Values may be sent and summed in bfloat16 or wider, within the bound.
No kernel may reach another device: no remote copies, remote signals or barrier semaphores. Data moves between devices by JAX's collectives and lax.ppermute only.
A program may use at most 320 MiB of HBM per device.

```python
import jax
import jax.numpy as jnp
from jax import lax

S = 1024
F = 512
SUB = 64
CHANNELS = 8192
BLOCK = 128
BLOCKS = 64
WINDOWS = 16
SLOTS = 2
OWNER_SLOTS = 64
PER_SLOT = 4


def pair_draw(key):
    inner = jax.random.fold_in(key, 7)
    key_start, key_perm, key_left, key_right, key_shuffle = jax.random.split(inner, 5)
    owner_count = OWNER_SLOTS // SLOTS
    quarter = owner_count // 4
    per_owner_slot = quarter // SLOTS
    per_device = BLOCKS // owner_count
    starts = jax.random.randint(key_start, (owner_count,), 0, owner_count // 2 + 1)
    starts = starts.at[0].set(owner_count // 2).at[1].set(0)
    owner_ids = jnp.arange(owner_count)
    orders = jax.vmap(lambda owner: jax.random.permutation(jax.random.fold_in(key_perm, owner), quarter))(owner_ids)
    left_device = starts[:, None] + orders
    right_device = left_device + quarter
    left_offset = jax.random.randint(key_left, (owner_count, quarter), 0, per_device)
    right_offset = jax.random.randint(key_right, (owner_count, quarter), 0, per_device)
    left_offset = left_offset.at[1].set(0)
    right_offset = right_offset.at[0].set(per_device - 1)
    first_block = left_device * per_device + left_offset
    second_block = right_device * per_device + right_offset
    slot_rows = owner_ids[:, None] * SLOTS + jnp.arange(quarter)[None, :] // per_owner_slot
    pair_rows = jnp.stack([first_block.reshape(-1), second_block.reshape(-1)], axis=1)
    shuffle = jax.random.permutation(key_shuffle, pair_rows.shape[0])
    return (pair_rows[shuffle].astype(jnp.int32), slot_rows.reshape(-1)[shuffle].astype(jnp.int32))


def draw_pair_list(key, part):
    return pair_draw(key)[0]


def draw_pair_owner(key, part):
    return pair_draw(key)[1]


def draw_traces(key, part):
    key_noise, key_channel, key_window = jax.random.split(key, 3)
    shape_all = (WINDOWS, CHANNELS, S)
    noise = jax.random.truncated_normal(key_noise, -6.0, 6.0, shape_all, jnp.float32)
    top_gain = 10.0
    channel_gain = jnp.exp(jax.random.uniform(key_channel, (1, CHANNELS, 1), jnp.float32, 0.0, jnp.log(top_gain)))
    window_gain = jnp.exp(jax.random.uniform(key_window, (WINDOWS, 1, 1), jnp.float32, 0.0, jnp.log(4.0)))
    return noise * channel_gain * window_gain


def setup_inputs(seed: int = 0) -> dict:
    key_list = jax.random.split(jax.random.key(seed), 4)
    traces = draw_traces(jax.random.fold_in(key_list[3], 71), 0)
    pair_list = draw_pair_list(jax.random.fold_in(key_list[3], 71), 0)
    pair_owner = draw_pair_owner(jax.random.fold_in(key_list[3], 71), 0)
    return {"traces": traces, "pair_list": pair_list, "pair_owner": pair_owner}


whiten_eps = 1e-05

def whiten(traces):
    spectra = jnp.fft.rfft(traces, axis=-1)[..., :F]
    real_part = jnp.real(spectra)
    imag_part = jnp.imag(spectra)
    shape_sub = traces.shape[:-1] + (F // SUB, SUB)
    real_band = real_part.reshape(shape_sub)
    imag_band = imag_part.reshape(shape_sub)
    band_power = lax.optimization_barrier(jnp.mean(real_band * real_band + imag_band * imag_band, axis=-1, keepdims=True))
    factor = lax.rsqrt(band_power + whiten_eps)
    stacked = jnp.stack([real_band * factor, imag_band * factor], axis=2)
    return stacked.reshape(traces.shape[:-1] + (2, F)).astype(jnp.bfloat16)

def reference(traces, pair_list, pair_owner):
    whitened = whiten(traces)
    order = jnp.argsort(pair_owner, stable=True)
    grouped = pair_list[order].reshape(OWNER_SLOTS, PER_SLOT, 2)

    def one_pair(blocks):
        start_left = (blocks[0] * BLOCK).astype(jnp.int32)
        start_right = (blocks[1] * BLOCK).astype(jnp.int32)
        left_rows = lax.dynamic_slice_in_dim(whitened, start_left, BLOCK, axis=1).astype(jnp.float32)
        right_rows = lax.dynamic_slice_in_dim(whitened, start_right, BLOCK, axis=1).astype(jnp.float32)
        rotated = jnp.stack([left_rows[:, :, 1], -left_rows[:, :, 0]], axis=2)
        paired = jnp.stack([left_rows, rotated], axis=1)
        return jnp.einsum('wcakf,wbkf->cabf', paired, right_rows)

    def one_slot(slot_pairs):

        def add_pair(step, total):
            return total + one_pair(slot_pairs[step])
        start = jnp.zeros((2, BLOCK, BLOCK, F), jnp.float32)
        return lax.fori_loop(0, PER_SLOT, add_pair, start).astype(jnp.bfloat16)
    return lax.map(one_slot, grouped)
```

```python
import jax
import jax.numpy as jnp
from jax import lax
from jax.sharding import PartitionSpec as P

SUB = 64
BLOCK = 128
SLOTS = 2
CHUNKS = 4


whiten_eps = 1e-05


def dft_table(samples, bin_count):
    sample_ids = lax.broadcasted_iota(jnp.int32, (samples, bin_count), 0)
    bin_ids = lax.broadcasted_iota(jnp.int32, (samples, bin_count), 1)
    phase_angle = (sample_ids * bin_ids % samples).astype(jnp.float32) * (2.0 * jnp.pi / samples)
    return jnp.concatenate([jnp.cos(phase_angle), -jnp.sin(phase_angle)], axis=1)


def whiten(flat_traces, bin_count):
    row_count, samples = flat_traces.shape
    spectra = jnp.dot(
        flat_traces,
        dft_table(samples, bin_count),
        precision=lax.Precision.HIGHEST,
        preferred_element_type=jnp.float32,
    )
    real_band = spectra[:, :bin_count].reshape(row_count, bin_count // SUB, SUB)
    imag_band = spectra[:, bin_count:].reshape(row_count, bin_count // SUB, SUB)
    band_power = jnp.mean(real_band * real_band + imag_band * imag_band, axis=-1, keepdims=True)
    factor = lax.rsqrt(band_power + whiten_eps)
    stacked = jnp.stack([real_band * factor, imag_band * factor], axis=1)
    return stacked.reshape(row_count, 2, bin_count).astype(jnp.bfloat16)


def slot_blocks(pair_list, pair_owner, slot_ids, per_slot):
    slot_match = (pair_owner[:, None] == slot_ids[None, :]).astype(jnp.int32)
    slot_rank = jnp.cumsum(slot_match, axis=0) - 1
    rank_ids = jnp.arange(per_slot, dtype=jnp.int32)
    selected = slot_match[:, :, None] * (slot_rank[:, :, None] == rank_ids[None, None, :]).astype(jnp.int32)
    first = jnp.sum(selected * pair_list[:, 0][:, None, None], axis=0)
    second = jnp.sum(selected * pair_list[:, 1][:, None, None], axis=0)
    return first, second


def shards(traces, pair_list, pair_owner):
    win_local, chan_local, samples = traces.shape
    bin_count = samples // 2
    bands = lax.axis_size("band")
    owners = lax.axis_size("pair")
    band_bins = bin_count // bands
    per_device = chan_local // BLOCK
    per_slot = pair_list.shape[0] // (owners * SLOTS)
    chunk = band_bins // CHUNKS

    whitened = whiten(traces.reshape(win_local * chan_local, samples), bin_count)
    whitened = whitened.reshape(win_local, per_device, BLOCK, 2, bands, band_bins)
    whitened = jnp.transpose(whitened, (4, 1, 3, 0, 5, 2))
    relaid = lax.all_to_all(whitened, "band", split_axis=0, concat_axis=0, tiled=True)

    device_index = lax.axis_index("pair")
    slot_ids = device_index * SLOTS + jnp.arange(SLOTS, dtype=jnp.int32)
    first, second = slot_blocks(pair_list, pair_owner, slot_ids, per_slot)

    out = jnp.zeros((SLOTS, 2, BLOCK, BLOCK, band_bins), jnp.bfloat16)
    for part in range(CHUNKS):
        piece = relaid[:, :, :, :, part * chunk:(part + 1) * chunk, :]
        gathered = lax.all_gather(piece, "pair", axis=1, tiled=True)
        left = jnp.take(gathered, first.reshape(-1), axis=1)
        left = left.reshape(left.shape[0], SLOTS, per_slot, *left.shape[2:])
        left = jnp.moveaxis(left, 1, 0)
        right = jnp.take(gathered, second.reshape(-1), axis=1)
        right = right.reshape(right.shape[0], SLOTS, per_slot, *right.shape[2:])
        right = jnp.moveaxis(right, 1, 0)
        rotated = jnp.stack([-right[:, :, :, 1], right[:, :, :, 0]], axis=3)
        paired = jnp.stack([right, rotated], axis=1)
        product = jnp.einsum(
            "sgtkwfa,spgtkwfb->spabf", left, paired, preferred_element_type=jnp.float32
        )
        out = lax.dynamic_update_slice_in_dim(out, product.astype(jnp.bfloat16), part * chunk, axis=4)
    return out


def solution(mesh):
    placed = (P("band", "pair", None), P(), P())
    return jax.shard_map(
        shards,
        mesh=mesh,
        in_specs=placed,
        out_specs=P("pair", None, None, None, "band"),
        check_vma=False,
    )
```

```python
import jax
import jax.numpy as jnp
from jax import lax
from jax.sharding import PartitionSpec as P

SUB = 64
BLOCK = 128
SLOTS = 2
CHUNKS = 8


whiten_eps = 1e-05


def dft_table(samples, bin_count):
    bin_ids = lax.broadcasted_iota(jnp.int32, (bin_count, samples), 0)
    sample_ids = lax.broadcasted_iota(jnp.int32, (bin_count, samples), 1)
    phase_angle = (sample_ids * bin_ids % samples).astype(jnp.float32) * (2.0 * jnp.pi / samples)
    return jnp.concatenate([jnp.cos(phase_angle), -jnp.sin(phase_angle)], axis=0)


def whiten(flat_traces, bin_count):
    row_count, samples = flat_traces.shape
    spectra = lax.dot_general(
        dft_table(samples, bin_count),
        flat_traces,
        (((1,), (1,)), ((), ())),
        precision=lax.Precision.HIGHEST,
        preferred_element_type=jnp.float32,
    )
    real_band = spectra[:bin_count].reshape(bin_count // SUB, SUB, row_count)
    imag_band = spectra[bin_count:].reshape(bin_count // SUB, SUB, row_count)
    band_power = jnp.mean(real_band * real_band + imag_band * imag_band, axis=1, keepdims=True)
    factor = lax.rsqrt(band_power + whiten_eps)
    stacked = jnp.stack([real_band * factor, imag_band * factor], axis=0)
    return stacked.reshape(2, bin_count, row_count).astype(jnp.bfloat16)


def slot_blocks(pair_list, pair_owner, slot_ids, per_slot):
    slot_match = (pair_owner[:, None] == slot_ids[None, :]).astype(jnp.int32)
    slot_rank = jnp.cumsum(slot_match, axis=0) - 1
    rank_ids = jnp.arange(per_slot, dtype=jnp.int32)
    selected = slot_match[:, :, None] * (slot_rank[:, :, None] == rank_ids[None, None, :]).astype(jnp.int32)
    first = jnp.sum(selected * pair_list[:, 0][:, None, None], axis=0)
    second = jnp.sum(selected * pair_list[:, 1][:, None, None], axis=0)
    return first, second


def shards(traces, pair_list, pair_owner):
    win_local, chan_local, samples = traces.shape
    bin_count = samples // 2
    bands = lax.axis_size("band")
    owners = lax.axis_size("pair")
    band_bins = bin_count // bands
    per_device = chan_local // BLOCK
    per_slot = pair_list.shape[0] // (owners * SLOTS)
    chunk = band_bins // CHUNKS

    whitened = whiten(traces.reshape(win_local * chan_local, samples), bin_count)
    whitened = whitened.reshape(2, bands, band_bins, win_local, per_device, BLOCK)
    whitened = jnp.transpose(whitened, (1, 4, 0, 3, 2, 5))
    relaid = lax.all_to_all(whitened, "band", split_axis=0, concat_axis=0, tiled=True)

    device_index = lax.axis_index("pair")
    slot_ids = device_index * SLOTS + jnp.arange(SLOTS, dtype=jnp.int32)
    first, second = slot_blocks(pair_list, pair_owner, slot_ids, per_slot)

    pieces = [relaid[:, :, :, :, part * chunk:(part + 1) * chunk, :] for part in range(CHUNKS)]
    out = jnp.zeros((SLOTS, 2, BLOCK, BLOCK, band_bins), jnp.bfloat16)
    for part in range(CHUNKS):
        piece = pieces[part]
        gathered = lax.all_gather(piece, "pair", axis=1, tiled=True)
        left = jnp.take(gathered, first.reshape(-1), axis=1)
        left = left.reshape(left.shape[0], SLOTS, per_slot, *left.shape[2:])
        left = jnp.moveaxis(left, 1, 0)
        right = jnp.take(gathered, second.reshape(-1), axis=1)
        right = right.reshape(right.shape[0], SLOTS, per_slot, *right.shape[2:])
        right = jnp.moveaxis(right, 1, 0)
        rotated = jnp.stack([-right[:, :, :, 1], right[:, :, :, 0]], axis=3)
        paired = jnp.stack([right, rotated], axis=1)
        product = jnp.einsum(
            "sgtkwfa,spgtkwfb->spabf", left, paired, preferred_element_type=jnp.float32
        )
        product = product.astype(jnp.bfloat16)
        if part + 2 < CHUNKS:
            pieces[part + 2], product = lax.optimization_barrier((pieces[part + 2], product))
        out = lax.dynamic_update_slice_in_dim(out, product, part * chunk, axis=4)
    return out


def solution(mesh):
    placed = (P("band", "pair", None), P(), P())
    return jax.shard_map(
        shards,
        mesh=mesh,
        in_specs=placed,
        out_specs=P("pair", None, None, None, "band"),
        check_vma=False,
    )
```

```python
import jax
import jax.numpy as jnp
from jax import lax
from jax.sharding import PartitionSpec as P
from jax.experimental.layout import Layout, with_layout_constraint

SUB = 64
BLOCK = 128
SLOTS = 2
CHUNKS = 4


whiten_eps = 1e-05


def dft_table(samples, bin_count):
    bin_ids = lax.broadcasted_iota(jnp.int32, (bin_count, samples), 0)
    sample_ids = lax.broadcasted_iota(jnp.int32, (bin_count, samples), 1)
    phase_angle = (sample_ids * bin_ids % samples).astype(jnp.float32) * (2.0 * jnp.pi / samples)
    return jnp.concatenate([jnp.cos(phase_angle), -jnp.sin(phase_angle)], axis=0)


def whiten(flat_traces, bin_count):
    row_count, samples = flat_traces.shape
    spectra = lax.dot_general(
        dft_table(samples, bin_count),
        flat_traces,
        (((1,), (1,)), ((), ())),
        precision=lax.Precision.HIGHEST,
        preferred_element_type=jnp.float32,
    )
    real_band = spectra[:bin_count].reshape(bin_count // SUB, SUB, row_count)
    imag_band = spectra[bin_count:].reshape(bin_count // SUB, SUB, row_count)
    band_power = jnp.mean(real_band * real_band + imag_band * imag_band, axis=1, keepdims=True)
    factor = lax.rsqrt(band_power + whiten_eps)
    stacked = jnp.stack([real_band * factor, imag_band * factor], axis=0)
    return stacked.reshape(2, bin_count, row_count).astype(jnp.bfloat16)


def slot_blocks(pair_list, pair_owner, slot_ids, per_slot):
    slot_match = (pair_owner[:, None] == slot_ids[None, :]).astype(jnp.int32)
    slot_rank = jnp.cumsum(slot_match, axis=0) - 1
    rank_ids = jnp.arange(per_slot, dtype=jnp.int32)
    selected = slot_match[:, :, None] * (slot_rank[:, :, None] == rank_ids[None, None, :]).astype(jnp.int32)
    first = jnp.sum(selected * pair_list[:, 0][:, None, None], axis=0)
    second = jnp.sum(selected * pair_list[:, 1][:, None, None], axis=0)
    return first, second


def shards(traces, pair_list, pair_owner):
    win_local, chan_local, samples = traces.shape
    bin_count = samples // 2
    bands = lax.axis_size("band")
    owners = lax.axis_size("pair")
    band_bins = bin_count // bands
    per_device = chan_local // BLOCK
    per_slot = pair_list.shape[0] // (owners * SLOTS)
    chunk = band_bins // CHUNKS

    whitened = whiten(traces.reshape(win_local * chan_local, samples), bin_count)
    whitened = whitened.reshape(2, bands, band_bins, win_local, per_device, BLOCK)
    whitened = jnp.transpose(whitened, (1, 4, 0, 3, 2, 5))
    relaid = lax.all_to_all(whitened, "band", split_axis=0, concat_axis=0, tiled=True)

    device_index = lax.axis_index("pair")
    slot_ids = device_index * SLOTS + jnp.arange(SLOTS, dtype=jnp.int32)
    first, second = slot_blocks(pair_list, pair_owner, slot_ids, per_slot)

    pieces = [
        jnp.transpose(relaid[:, :, :, :, part * chunk:(part + 1) * chunk, :], (1, 0, 2, 3, 4, 5))
        for part in range(CHUNKS)
    ]
    out = jnp.zeros((SLOTS, 2, BLOCK, BLOCK, band_bins), jnp.bfloat16)
    for part in range(CHUNKS):
        piece = pieces[part]
        gathered = lax.all_gather(piece, "pair", axis=0, tiled=True)
        left = jnp.take(gathered, first.reshape(-1), axis=0)
        left = left.reshape(SLOTS, per_slot, *left.shape[1:])
        right = jnp.take(gathered, second.reshape(-1), axis=0)
        right = right.reshape(SLOTS, per_slot, *right.shape[1:])
        rotated = jnp.stack([-right[:, :, :, 1], right[:, :, :, 0]], axis=3)
        paired = jnp.stack([right, rotated], axis=1)
        product = jnp.einsum(
            "stgkwfa,sptgkwfb->spabf", left, paired, preferred_element_type=jnp.float32
        )
        product = with_layout_constraint(product.astype(jnp.bfloat16), Layout((0, 1, 2, 3, 4)))
        if part + 2 < CHUNKS:
            pieces[part + 2], product = lax.optimization_barrier((pieces[part + 2], product))
        out = lax.dynamic_update_slice_in_dim(out, product, part * chunk, axis=4)
    return out


def solution(mesh):
    placed = (P("band", "pair", None), P(), P())
    return jax.shard_map(
        shards,
        mesh=mesh,
        in_specs=placed,
        out_specs=P("pair", None, None, None, "band"),
        check_vma=False,
    )
```

```python
import jax
import jax.numpy as jnp
from jax import lax
from jax.sharding import PartitionSpec as P

SUB = 64
BLOCK = 128
SLOTS = 2
CHUNKS = 4


whiten_eps = 1e-05


def dft_table(samples, bin_count):
    bin_ids = lax.broadcasted_iota(jnp.int32, (bin_count, samples), 0)
    sample_ids = lax.broadcasted_iota(jnp.int32, (bin_count, samples), 1)
    phase_angle = (sample_ids * bin_ids % samples).astype(jnp.float32) * (2.0 * jnp.pi / samples)
    return jnp.concatenate([jnp.cos(phase_angle), -jnp.sin(phase_angle)], axis=0)


def whiten(flat_traces, bin_count):
    row_count, samples = flat_traces.shape
    spectra = lax.dot_general(
        dft_table(samples, bin_count),
        flat_traces,
        (((1,), (1,)), ((), ())),
        precision=lax.Precision.HIGHEST,
        preferred_element_type=jnp.float32,
    )
    real_band = spectra[:bin_count].reshape(bin_count // SUB, SUB, row_count)
    imag_band = spectra[bin_count:].reshape(bin_count // SUB, SUB, row_count)
    band_power = jnp.mean(real_band * real_band + imag_band * imag_band, axis=1, keepdims=True)
    factor = lax.rsqrt(band_power + whiten_eps)
    stacked = jnp.stack([real_band * factor, imag_band * factor], axis=0)
    return stacked.reshape(2, bin_count, row_count).astype(jnp.bfloat16)


def slot_blocks(pair_list, pair_owner, slot_ids, per_slot):
    slot_match = (pair_owner[:, None] == slot_ids[None, :]).astype(jnp.int32)
    slot_rank = jnp.cumsum(slot_match, axis=0) - 1
    rank_ids = jnp.arange(per_slot, dtype=jnp.int32)
    selected = slot_match[:, :, None] * (slot_rank[:, :, None] == rank_ids[None, None, :]).astype(jnp.int32)
    first = jnp.sum(selected * pair_list[:, 0][:, None, None], axis=0)
    second = jnp.sum(selected * pair_list[:, 1][:, None, None], axis=0)
    return first, second


def shards(traces, pair_list, pair_owner):
    win_local, chan_local, samples = traces.shape
    bin_count = samples // 2
    bands = lax.axis_size("band")
    owners = lax.axis_size("pair")
    band_bins = bin_count // bands
    per_device = chan_local // BLOCK
    per_slot = pair_list.shape[0] // (owners * SLOTS)
    chunk = band_bins // CHUNKS

    whitened = whiten(traces.reshape(win_local * chan_local, samples), bin_count)
    whitened = whitened.reshape(2, bands, band_bins, win_local, per_device, BLOCK)
    whitened = jnp.transpose(whitened, (1, 4, 0, 3, 2, 5))

    device_index = lax.axis_index("pair")
    slot_ids = device_index * SLOTS + jnp.arange(SLOTS, dtype=jnp.int32)
    first, second = slot_blocks(pair_list, pair_owner, slot_ids, per_slot)

    pieces = [
        lax.all_to_all(
            whitened[:, :, :, :, part * chunk:(part + 1) * chunk, :], "band", split_axis=0, concat_axis=0, tiled=True
        )
        for part in range(CHUNKS)
    ]
    out = jnp.zeros((SLOTS, 2, BLOCK, BLOCK, band_bins), jnp.bfloat16)
    for part in range(CHUNKS):
        gathered = lax.all_gather(pieces[part], "pair", axis=1, tiled=True)
        left = jnp.take(gathered, first.reshape(-1), axis=1)
        left = left.reshape(left.shape[0], SLOTS, per_slot, *left.shape[2:])
        left = jnp.moveaxis(left, 1, 0)
        right = jnp.take(gathered, second.reshape(-1), axis=1)
        right = right.reshape(right.shape[0], SLOTS, per_slot, *right.shape[2:])
        right = jnp.moveaxis(right, 1, 0)
        rotated = jnp.stack([-right[:, :, :, 1], right[:, :, :, 0]], axis=3)
        paired = jnp.stack([right, rotated], axis=1)
        product = jnp.einsum(
            "sgtkwfa,spgtkwfb->spabf", left, paired, preferred_element_type=jnp.float32
        )
        product = product.astype(jnp.bfloat16)
        if part + 2 < CHUNKS:
            pieces[part + 2], product = lax.optimization_barrier((pieces[part + 2], product))
        out = lax.dynamic_update_slice_in_dim(out, product, part * chunk, axis=4)
    return out


def solution(mesh):
    placed = (P("band", "pair", None), P(), P())
    return jax.shard_map(
        shards,
        mesh=mesh,
        in_specs=placed,
        out_specs=P("pair", None, None, None, "band"),
        check_vma=False,
    )
```

```python
import jax
import jax.numpy as jnp
from jax import lax
from jax.sharding import PartitionSpec as P

SUB = 64
BLOCK = 128
SLOTS = 2
CHUNKS = 4


whiten_eps = 1e-05


def dft_table(samples, bin_count):
    bin_ids = lax.broadcasted_iota(jnp.int32, (bin_count, samples), 0)
    sample_ids = lax.broadcasted_iota(jnp.int32, (bin_count, samples), 1)
    phase_angle = (sample_ids * bin_ids % samples).astype(jnp.float32) * (2.0 * jnp.pi / samples)
    return jnp.concatenate([jnp.cos(phase_angle), -jnp.sin(phase_angle)], axis=0)


def whiten(flat_traces, bin_count):
    row_count, samples = flat_traces.shape
    spectra = lax.dot_general(
        dft_table(samples, bin_count),
        flat_traces,
        (((1,), (1,)), ((), ())),
        precision=lax.Precision.HIGHEST,
        preferred_element_type=jnp.float32,
    )
    real_band = spectra[:bin_count].reshape(bin_count // SUB, SUB, row_count)
    imag_band = spectra[bin_count:].reshape(bin_count // SUB, SUB, row_count)
    band_power = jnp.mean(real_band * real_band + imag_band * imag_band, axis=1, keepdims=True)
    factor = lax.rsqrt(band_power + whiten_eps)
    stacked = jnp.stack([real_band * factor, imag_band * factor], axis=0)
    return stacked.reshape(2, bin_count, row_count).astype(jnp.bfloat16)


def slot_blocks(pair_list, pair_owner, slot_ids, per_slot):
    slot_match = (pair_owner[:, None] == slot_ids[None, :]).astype(jnp.int32)
    slot_rank = jnp.cumsum(slot_match, axis=0) - 1
    rank_ids = jnp.arange(per_slot, dtype=jnp.int32)
    selected = slot_match[:, :, None] * (slot_rank[:, :, None] == rank_ids[None, None, :]).astype(jnp.int32)
    first = jnp.sum(selected * pair_list[:, 0][:, None, None], axis=0)
    second = jnp.sum(selected * pair_list[:, 1][:, None, None], axis=0)
    return first, second


def shards(traces, pair_list, pair_owner):
    win_local, chan_local, samples = traces.shape
    bin_count = samples // 2
    bands = lax.axis_size("band")
    owners = lax.axis_size("pair")
    band_bins = bin_count // bands
    per_device = chan_local // BLOCK
    per_slot = pair_list.shape[0] // (owners * SLOTS)
    chunk = band_bins // CHUNKS

    whitened = whiten(traces.reshape(win_local * chan_local, samples), bin_count)
    whitened = whitened.reshape(2, bands, band_bins, win_local, per_device, BLOCK)
    whitened = jnp.transpose(whitened, (1, 4, 0, 3, 2, 5))

    device_index = lax.axis_index("pair")
    slot_ids = device_index * SLOTS + jnp.arange(SLOTS, dtype=jnp.int32)
    first, second = slot_blocks(pair_list, pair_owner, slot_ids, per_slot)

    pieces = [
        lax.all_to_all(
            whitened[:, :, :, :, part * chunk:(part + 1) * chunk, :], "band", split_axis=0, concat_axis=0, tiled=True
        )
        for part in range(CHUNKS)
    ]
    wanted = jnp.concatenate([first.reshape(-1), second.reshape(-1)])
    picks = (wanted[:, None] == jnp.arange(owners * per_device, dtype=jnp.int32)[None, :]).astype(jnp.bfloat16)
    out = jnp.zeros((SLOTS, 2, BLOCK, BLOCK, band_bins), jnp.bfloat16)
    for part in range(CHUNKS):
        piece = jnp.transpose(pieces[part], (1, 0, 2, 3, 4, 5))
        gathered = lax.all_gather(piece, "pair", axis=0, tiled=True)
        rows = gathered.shape[0]
        chosen = jnp.dot(picks, gathered.reshape(rows, -1), preferred_element_type=jnp.bfloat16)
        chosen = chosen.reshape(2, SLOTS, per_slot, *gathered.shape[1:])
        left = chosen[0]
        right = chosen[1]
        rotated = jnp.stack([-right[:, :, :, 1], right[:, :, :, 0]], axis=3)
        paired = jnp.stack([right, rotated], axis=1)
        product = jnp.einsum(
            "stgkwfa,sptgkwfb->spabf", left, paired, preferred_element_type=jnp.float32
        )
        product = product.astype(jnp.bfloat16)
        if part + 2 < CHUNKS:
            pieces[part + 2], product = lax.optimization_barrier((pieces[part + 2], product))
        out = lax.dynamic_update_slice_in_dim(out, product, part * chunk, axis=4)
    return out


def solution(mesh):
    placed = (P("band", "pair", None), P(), P())
    return jax.shard_map(
        shards,
        mesh=mesh,
        in_specs=placed,
        out_specs=P("pair", None, None, None, "band"),
        check_vma=False,
    )
```

```python
import jax
import jax.numpy as jnp
from jax import lax
from jax.sharding import Mesh, PartitionSpec as P

SUB = 64
BLOCK = 128
SLOTS = 2
CHUNKS = 4


whiten_eps = 1e-05


def dft_table(samples, bin_count):
    bin_ids = lax.broadcasted_iota(jnp.int32, (bin_count, samples), 0)
    sample_ids = lax.broadcasted_iota(jnp.int32, (bin_count, samples), 1)
    phase_angle = (sample_ids * bin_ids % samples).astype(jnp.float32) * (2.0 * jnp.pi / samples)
    return jnp.concatenate([jnp.cos(phase_angle), -jnp.sin(phase_angle)], axis=0)


def whiten(flat_traces, bin_count):
    row_count, samples = flat_traces.shape
    spectra = lax.dot_general(
        dft_table(samples, bin_count),
        flat_traces,
        (((1,), (1,)), ((), ())),
        precision=lax.Precision.HIGHEST,
        preferred_element_type=jnp.float32,
    )
    real_band = spectra[:bin_count].reshape(bin_count // SUB, SUB, row_count)
    imag_band = spectra[bin_count:].reshape(bin_count // SUB, SUB, row_count)
    band_power = jnp.mean(real_band * real_band + imag_band * imag_band, axis=1, keepdims=True)
    factor = lax.rsqrt(band_power + whiten_eps)
    stacked = jnp.stack([real_band * factor, imag_band * factor], axis=0)
    return stacked.reshape(2, bin_count, row_count).astype(jnp.bfloat16)


def slot_blocks(pair_list, pair_owner, slot_ids, per_slot):
    slot_match = (pair_owner[:, None] == slot_ids[None, :]).astype(jnp.int32)
    slot_rank = jnp.cumsum(slot_match, axis=0) - 1
    rank_ids = jnp.arange(per_slot, dtype=jnp.int32)
    selected = slot_match[:, :, None] * (slot_rank[:, :, None] == rank_ids[None, None, :]).astype(jnp.int32)
    first = jnp.sum(selected * pair_list[:, 0][:, None, None], axis=0)
    second = jnp.sum(selected * pair_list[:, 1][:, None, None], axis=0)
    return first, second


def shards(traces, pair_list, pair_owner):
    win_local, chan_local, samples = traces.shape
    bin_count = samples // 2
    bands = lax.axis_size("band")
    cores = lax.axis_size("core")
    owners = lax.axis_size("chip") * cores
    band_bins = bin_count // bands
    per_device = chan_local // BLOCK
    per_slot = pair_list.shape[0] // (owners * SLOTS)
    chunk = band_bins // CHUNKS

    whitened = whiten(traces.reshape(win_local * chan_local, samples), bin_count)
    whitened = whitened.reshape(2, bands, band_bins, win_local, per_device, BLOCK)
    whitened = jnp.transpose(whitened, (1, 4, 0, 3, 2, 5))

    core = lax.axis_index("core")
    device_index = lax.axis_index("chip") * cores + core
    slot_ids = device_index * SLOTS + jnp.arange(SLOTS, dtype=jnp.int32)
    first, second = slot_blocks(pair_list, pair_owner, slot_ids, per_slot)

    pieces = [
        lax.all_to_all(
            whitened[:, :, :, :, part * chunk:(part + 1) * chunk, :], "band", split_axis=0, concat_axis=0, tiled=True
        )
        for part in range(CHUNKS)
    ]
    wanted = jnp.concatenate([first.reshape(-1), second.reshape(-1)])
    block_core = (wanted // per_device) % cores
    column = (wanted // (per_device * cores)) * per_device + wanted % per_device
    half = owners * per_device // cores
    spots = jnp.arange(half, dtype=jnp.int32)[None, :]
    own_picks = ((column[:, None] == spots) & (block_core[:, None] == core)).astype(jnp.bfloat16)
    other_picks = ((column[:, None] == spots) & (block_core[:, None] != core)).astype(jnp.bfloat16)
    swap = [(i, i ^ 1) for i in range(cores)]
    out = jnp.zeros((SLOTS, 2, BLOCK, BLOCK, band_bins), jnp.bfloat16)
    for part in range(CHUNKS):
        piece = jnp.transpose(pieces[part], (1, 0, 2, 3, 4, 5))
        gathered = lax.all_gather(piece, "chip", axis=0, tiled=True)
        other = lax.ppermute(gathered, "core", swap)
        rows = gathered.shape[0]
        chosen = jnp.dot(own_picks, gathered.reshape(rows, -1), preferred_element_type=jnp.float32)
        chosen = chosen + jnp.dot(other_picks, other.reshape(rows, -1), preferred_element_type=jnp.float32)
        chosen = chosen.astype(jnp.bfloat16)
        chosen = chosen.reshape(2, SLOTS, per_slot, *gathered.shape[1:])
        left = chosen[0]
        right = chosen[1]
        rotated = jnp.stack([-right[:, :, :, 1], right[:, :, :, 0]], axis=3)
        paired = jnp.stack([right, rotated], axis=1)
        product = jnp.einsum(
            "stgkwfa,sptgkwfb->spabf", left, paired, preferred_element_type=jnp.float32
        )
        product = product.astype(jnp.bfloat16)
        if part + 2 < CHUNKS:
            pieces[part + 2], product = lax.optimization_barrier((pieces[part + 2], product))
        out = lax.dynamic_update_slice_in_dim(out, product, part * chunk, axis=4)
    return out


def solution(mesh):
    band_count, pair_count = mesh.devices.shape
    cores = 2
    split = Mesh(mesh.devices.reshape(band_count, pair_count // cores, cores), ("band", "chip", "core"))
    placed = (P("band", ("chip", "core"), None), P(), P())
    return jax.shard_map(
        shards,
        mesh=split,
        in_specs=placed,
        out_specs=P(("chip", "core"), None, None, None, "band"),
        check_vma=False,
    )
```

```python
import jax
import jax.numpy as jnp
from jax import lax
from jax.sharding import PartitionSpec as P

SUB = 64
BLOCK = 128
SLOTS = 2
CHUNKS = 4


whiten_eps = 1e-05


def dft_table(samples, bins):
    bin_ids = jnp.broadcast_to(bins[:, None], (bins.shape[0], samples))
    sample_ids = lax.broadcasted_iota(jnp.int32, (bins.shape[0], samples), 1)
    phase_angle = (sample_ids * bin_ids % samples).astype(jnp.float32) * (2.0 * jnp.pi / samples)
    return jnp.concatenate([jnp.cos(phase_angle), -jnp.sin(phase_angle)], axis=0)


def whiten(flat_traces, bins):
    row_count, samples = flat_traces.shape
    bin_count = bins.shape[0]
    spectra = lax.dot_general(
        dft_table(samples, bins),
        flat_traces,
        (((1,), (1,)), ((), ())),
        precision=lax.Precision.HIGHEST,
        preferred_element_type=jnp.float32,
    )
    real_band = spectra[:bin_count].reshape(bin_count // SUB, SUB, row_count)
    imag_band = spectra[bin_count:].reshape(bin_count // SUB, SUB, row_count)
    band_power = jnp.mean(real_band * real_band + imag_band * imag_band, axis=1, keepdims=True)
    factor = lax.rsqrt(band_power + whiten_eps)
    stacked = jnp.stack([real_band * factor, imag_band * factor], axis=0)
    return stacked.reshape(2, bin_count, row_count).astype(jnp.bfloat16)


def slot_blocks(pair_list, pair_owner, slot_ids, per_slot):
    slot_match = (pair_owner[:, None] == slot_ids[None, :]).astype(jnp.int32)
    slot_rank = jnp.cumsum(slot_match, axis=0) - 1
    rank_ids = jnp.arange(per_slot, dtype=jnp.int32)
    selected = slot_match[:, :, None] * (slot_rank[:, :, None] == rank_ids[None, None, :]).astype(jnp.int32)
    first = jnp.sum(selected * pair_list[:, 0][:, None, None], axis=0)
    second = jnp.sum(selected * pair_list[:, 1][:, None, None], axis=0)
    return first, second


def shards(traces, pair_list, pair_owner):
    win_local, chan_local, samples = traces.shape
    bin_count = samples // 2
    bands = lax.axis_size("band")
    owners = lax.axis_size("pair")
    band_bins = bin_count // bands
    per_device = chan_local // BLOCK
    per_slot = pair_list.shape[0] // (owners * SLOTS)
    chunk = band_bins // CHUNKS

    flat = traces.reshape(win_local * chan_local, samples)
    halves = 2
    half_bins = band_bins // halves
    per_half = CHUNKS // halves
    pieces = []
    for half in range(halves):
        ids = jnp.arange(bands * half_bins, dtype=jnp.int32)
        bins = (ids // half_bins) * band_bins + half * half_bins + ids % half_bins
        whitened = whiten(flat, bins)
        whitened = whitened.reshape(2, bands, half_bins, win_local, per_device, BLOCK)
        whitened = jnp.transpose(whitened, (1, 4, 0, 3, 2, 5))
        for part in range(per_half):
            pieces.append(
                lax.all_to_all(
                    whitened[:, :, :, :, part * chunk:(part + 1) * chunk, :],
                    "band", split_axis=0, concat_axis=0, tiled=True,
                )
            )

    device_index = lax.axis_index("pair")
    slot_ids = device_index * SLOTS + jnp.arange(SLOTS, dtype=jnp.int32)
    first, second = slot_blocks(pair_list, pair_owner, slot_ids, per_slot)

    wanted = jnp.concatenate([first.reshape(-1), second.reshape(-1)])
    picks = (wanted[:, None] == jnp.arange(owners * per_device, dtype=jnp.int32)[None, :]).astype(jnp.bfloat16)
    out = jnp.zeros((SLOTS, 2, BLOCK, BLOCK, band_bins), jnp.bfloat16)
    for part in range(CHUNKS):
        piece = jnp.transpose(pieces[part], (1, 0, 2, 3, 4, 5))
        gathered = lax.all_gather(piece, "pair", axis=0, tiled=True)
        rows = gathered.shape[0]
        chosen = jnp.dot(picks, gathered.reshape(rows, -1), preferred_element_type=jnp.bfloat16)
        chosen = chosen.reshape(2, SLOTS, per_slot, *gathered.shape[1:])
        left = chosen[0]
        right = chosen[1]
        rotated = jnp.stack([-right[:, :, :, 1], right[:, :, :, 0]], axis=3)
        paired = jnp.stack([right, rotated], axis=1)
        product = jnp.einsum(
            "stgkwfa,sptgkwfb->spabf", left, paired, preferred_element_type=jnp.float32
        )
        product = product.astype(jnp.bfloat16)
        if part + 2 < CHUNKS:
            pieces[part + 2], product = lax.optimization_barrier((pieces[part + 2], product))
        out = lax.dynamic_update_slice_in_dim(out, product, part * chunk, axis=4)
    return out


def solution(mesh):
    placed = (P("band", "pair", None), P(), P())
    return jax.shard_map(
        shards,
        mesh=mesh,
        in_specs=placed,
        out_specs=P("pair", None, None, None, "band"),
        check_vma=False,
    )
```

```python
import jax
import jax.numpy as jnp
from jax import lax
from jax.sharding import PartitionSpec as P

SUB = 64
BLOCK = 128
SLOTS = 2
CHUNKS = 4


whiten_eps = 1e-05


def dft_table(samples, bins):
    bin_ids = jnp.broadcast_to(bins[:, None], (bins.shape[0], samples))
    sample_ids = lax.broadcasted_iota(jnp.int32, (bins.shape[0], samples), 1)
    phase_angle = (sample_ids * bin_ids % samples).astype(jnp.float32) * (2.0 * jnp.pi / samples)
    return jnp.concatenate([jnp.cos(phase_angle), -jnp.sin(phase_angle)], axis=0)


def whiten(flat_traces, bins):
    row_count, samples = flat_traces.shape
    bin_count = bins.shape[0]
    spectra = lax.dot_general(
        dft_table(samples, bins),
        flat_traces,
        (((1,), (1,)), ((), ())),
        precision=lax.Precision.HIGH,
        preferred_element_type=jnp.float32,
    )
    real_band = spectra[:bin_count].reshape(bin_count // SUB, SUB, row_count)
    imag_band = spectra[bin_count:].reshape(bin_count // SUB, SUB, row_count)
    band_power = jnp.mean(real_band * real_band + imag_band * imag_band, axis=1, keepdims=True)
    factor = lax.rsqrt(band_power + whiten_eps)
    stacked = jnp.stack([real_band * factor, imag_band * factor], axis=0)
    return stacked.reshape(2, bin_count, row_count).astype(jnp.bfloat16)


def slot_blocks(pair_list, pair_owner, slot_ids, per_slot):
    slot_match = (pair_owner[:, None] == slot_ids[None, :]).astype(jnp.int32)
    slot_rank = jnp.cumsum(slot_match, axis=0) - 1
    rank_ids = jnp.arange(per_slot, dtype=jnp.int32)
    selected = slot_match[:, :, None] * (slot_rank[:, :, None] == rank_ids[None, None, :]).astype(jnp.int32)
    first = jnp.sum(selected * pair_list[:, 0][:, None, None], axis=0)
    second = jnp.sum(selected * pair_list[:, 1][:, None, None], axis=0)
    return first, second


def shards(traces, pair_list, pair_owner):
    win_local, chan_local, samples = traces.shape
    bin_count = samples // 2
    bands = lax.axis_size("band")
    owners = lax.axis_size("pair")
    band_bins = bin_count // bands
    per_device = chan_local // BLOCK
    per_slot = pair_list.shape[0] // (owners * SLOTS)
    chunk = band_bins // CHUNKS

    flat = traces.reshape(win_local * chan_local, samples)
    halves = 2
    half_bins = band_bins // halves
    per_half = CHUNKS // halves
    pieces = []
    for half in range(halves):
        ids = jnp.arange(bands * half_bins, dtype=jnp.int32)
        bins = (ids // half_bins) * band_bins + half * half_bins + ids % half_bins
        whitened = whiten(flat, bins)
        whitened = whitened.reshape(2, bands, half_bins, win_local, per_device, BLOCK)
        whitened = jnp.transpose(whitened, (1, 4, 0, 3, 2, 5))
        for part in range(per_half):
            pieces.append(
                lax.all_to_all(
                    whitened[:, :, :, :, part * chunk:(part + 1) * chunk, :],
                    "band", split_axis=0, concat_axis=0, tiled=True,
                )
            )

    device_index = lax.axis_index("pair")
    slot_ids = device_index * SLOTS + jnp.arange(SLOTS, dtype=jnp.int32)
    first, second = slot_blocks(pair_list, pair_owner, slot_ids, per_slot)

    wanted = jnp.concatenate([first.reshape(-1), second.reshape(-1)])
    picks = (wanted[:, None] == jnp.arange(owners * per_device, dtype=jnp.int32)[None, :]).astype(jnp.bfloat16)
    products = []
    for part in range(CHUNKS):
        piece = jnp.transpose(pieces[part], (1, 0, 2, 3, 4, 5))
        gathered = lax.all_gather(piece, "pair", axis=0, tiled=True)
        if part == CHUNKS - 1 and part >= 1:
            gathered, products[-1] = lax.optimization_barrier((gathered, products[-1]))
        rows = gathered.shape[0]
        chosen = jnp.dot(picks, gathered.reshape(rows, -1), preferred_element_type=jnp.bfloat16)
        chosen = chosen.reshape(2, SLOTS, per_slot, *gathered.shape[1:])
        left = chosen[0]
        right = chosen[1]
        rotated = jnp.stack([-right[:, :, :, 1], right[:, :, :, 0]], axis=3)
        paired = jnp.stack([right, rotated], axis=1)
        product = jnp.einsum(
            "stgkwfa,sptgkwfb->spabf", left, paired, preferred_element_type=jnp.float32
        )
        product = product.astype(jnp.bfloat16)
        if part + 2 < CHUNKS:
            pieces[part + 2], product = lax.optimization_barrier((pieces[part + 2], product))
        products.append(product)
    out = jnp.zeros((SLOTS, 2, BLOCK, BLOCK, band_bins), jnp.bfloat16)
    for part in range(CHUNKS):
        out = lax.dynamic_update_slice_in_dim(out, products[part], part * chunk, axis=4)
    return out


def solution(mesh):
    placed = (P("band", "pair", None), P(), P())
    return jax.shard_map(
        shards,
        mesh=mesh,
        in_specs=placed,
        out_specs=P("pair", None, None, None, "band"),
        check_vma=False,
    )
```

```python
import jax
import jax.numpy as jnp
from jax import lax
from jax.sharding import PartitionSpec as P

SUB = 64
BLOCK = 128
SLOTS = 2


whiten_eps = 1e-05


def dft_table(samples, bins):
    bin_ids = jnp.broadcast_to(bins[:, None], (bins.shape[0], samples))
    sample_ids = lax.broadcasted_iota(jnp.int32, (bins.shape[0], samples), 1)
    phase_angle = (sample_ids * bin_ids % samples).astype(jnp.float32) * (2.0 * jnp.pi / samples)
    return jnp.concatenate([jnp.cos(phase_angle), -jnp.sin(phase_angle)], axis=0)


def whiten(flat_traces, bins):
    row_count, samples = flat_traces.shape
    bin_count = bins.shape[0]
    spectra = lax.dot_general(
        dft_table(samples, bins),
        flat_traces,
        (((1,), (1,)), ((), ())),
        precision=lax.Precision.HIGH,
        preferred_element_type=jnp.float32,
    )
    real_band = spectra[:bin_count].reshape(bin_count // SUB, SUB, row_count)
    imag_band = spectra[bin_count:].reshape(bin_count // SUB, SUB, row_count)
    band_power = jnp.mean(real_band * real_band + imag_band * imag_band, axis=1, keepdims=True)
    factor = lax.rsqrt(band_power + whiten_eps)
    stacked = jnp.stack([real_band * factor, imag_band * factor], axis=0)
    return stacked.reshape(2, bin_count, row_count).astype(jnp.bfloat16)


def slot_blocks(pair_list, pair_owner, slot_ids, per_slot):
    slot_match = (pair_owner[:, None] == slot_ids[None, :]).astype(jnp.int32)
    slot_rank = jnp.cumsum(slot_match, axis=0) - 1
    rank_ids = jnp.arange(per_slot, dtype=jnp.int32)
    selected = slot_match[:, :, None] * (slot_rank[:, :, None] == rank_ids[None, None, :]).astype(jnp.int32)
    first = jnp.sum(selected * pair_list[:, 0][:, None, None], axis=0)
    second = jnp.sum(selected * pair_list[:, 1][:, None, None], axis=0)
    return first, second


def shards(traces, pair_list, pair_owner):
    win_local, chan_local, samples = traces.shape
    bin_count = samples // 2
    bands = lax.axis_size("band")
    owners = lax.axis_size("pair")
    band_bins = bin_count // bands
    per_device = chan_local // BLOCK
    per_slot = pair_list.shape[0] // (owners * SLOTS)

    flat = traces.reshape(win_local * chan_local, samples)
    halves = 2
    half_bins = band_bins // halves
    edges = [0, 3 * band_bins // 8, 6 * band_bins // 8, band_bins]
    spans = []
    for half in range(halves):
        ids = jnp.arange(bands * half_bins, dtype=jnp.int32)
        bins = (ids // half_bins) * band_bins + half * half_bins + ids % half_bins
        whitened = whiten(flat, bins)
        whitened = whitened.reshape(2, bands, half_bins, win_local, per_device, BLOCK)
        spans.append(jnp.transpose(whitened, (1, 4, 0, 3, 2, 5)))
    pieces = []
    for low, high in zip(edges[:-1], edges[1:]):
        parts = []
        for half in range(halves):
            start = max(low, half * half_bins)
            stop = min(high, (half + 1) * half_bins)
            if start < stop:
                parts.append(spans[half][:, :, :, :, start - half * half_bins:stop - half * half_bins, :])
        chunk_bins = parts[0] if len(parts) == 1 else jnp.concatenate(parts, axis=4)
        pieces.append(lax.all_to_all(chunk_bins, "band", split_axis=0, concat_axis=0, tiled=True))
    chunks = len(pieces)

    device_index = lax.axis_index("pair")
    slot_ids = device_index * SLOTS + jnp.arange(SLOTS, dtype=jnp.int32)
    first, second = slot_blocks(pair_list, pair_owner, slot_ids, per_slot)

    wanted = jnp.concatenate([first.reshape(-1), second.reshape(-1)])
    picks = (wanted[:, None] == jnp.arange(owners * per_device, dtype=jnp.int32)[None, :]).astype(jnp.bfloat16)
    products = []
    for part in range(chunks):
        piece = jnp.transpose(pieces[part], (1, 0, 2, 3, 4, 5))
        gathered = lax.all_gather(piece, "pair", axis=0, tiled=True)
        if part == chunks - 1 and part >= 1:
            gathered, products[-1] = lax.optimization_barrier((gathered, products[-1]))
        rows = gathered.shape[0]
        chosen = jnp.dot(picks, gathered.reshape(rows, -1), preferred_element_type=jnp.bfloat16)
        chosen = chosen.reshape(2, SLOTS, per_slot, *gathered.shape[1:])
        left = chosen[0]
        right = chosen[1]
        rotated = jnp.stack([-right[:, :, :, 1], right[:, :, :, 0]], axis=3)
        paired = jnp.stack([right, rotated], axis=1)
        product = jnp.einsum(
            "stgkwfa,sptgkwfb->spabf", left, paired, preferred_element_type=jnp.float32
        )
        product = product.astype(jnp.bfloat16)
        if part + 2 < chunks:
            pieces[part + 2], product = lax.optimization_barrier((pieces[part + 2], product))
        products.append(product)
    out = jnp.zeros((SLOTS, 2, BLOCK, BLOCK, band_bins), jnp.bfloat16)
    for part in range(chunks):
        out = lax.dynamic_update_slice_in_dim(out, products[part], edges[part], axis=4)
    return out


def solution(mesh):
    placed = (P("band", "pair", None), P(), P())
    return jax.shard_map(
        shards,
        mesh=mesh,
        in_specs=placed,
        out_specs=P("pair", None, None, None, "band"),
        check_vma=False,
    )
```

```python
import jax
import jax.numpy as jnp
from jax import lax
from jax.sharding import PartitionSpec as P

SUB = 64
BLOCK = 128
SLOTS = 2


whiten_eps = 1e-05


def dft_table(samples, bins):
    bin_ids = jnp.broadcast_to(bins[:, None], (bins.shape[0], samples))
    sample_ids = lax.broadcasted_iota(jnp.int32, (bins.shape[0], samples), 1)
    phase_angle = (sample_ids * bin_ids % samples).astype(jnp.float32) * (2.0 * jnp.pi / samples)
    return jnp.concatenate([jnp.cos(phase_angle), -jnp.sin(phase_angle)], axis=0)


def whiten(flat_traces, bins):
    row_count, samples = flat_traces.shape
    bin_count = bins.shape[0]
    spectra = lax.dot_general(
        dft_table(samples, bins),
        flat_traces,
        (((1,), (1,)), ((), ())),
        precision=lax.Precision.HIGH,
        preferred_element_type=jnp.float32,
    )
    real_band = spectra[:bin_count].reshape(bin_count // SUB, SUB, row_count)
    imag_band = spectra[bin_count:].reshape(bin_count // SUB, SUB, row_count)
    band_power = jnp.mean(real_band * real_band + imag_band * imag_band, axis=1, keepdims=True)
    factor = lax.rsqrt(band_power + whiten_eps)
    stacked = jnp.stack([real_band * factor, imag_band * factor], axis=0)
    return stacked.reshape(2, bin_count, row_count).astype(jnp.bfloat16)


def slot_blocks(pair_list, pair_owner, slot_ids, per_slot):
    slot_match = (pair_owner[:, None] == slot_ids[None, :]).astype(jnp.int32)
    slot_rank = jnp.cumsum(slot_match, axis=0) - 1
    rank_ids = jnp.arange(per_slot, dtype=jnp.int32)
    selected = slot_match[:, :, None] * (slot_rank[:, :, None] == rank_ids[None, None, :]).astype(jnp.int32)
    first = jnp.sum(selected * pair_list[:, 0][:, None, None], axis=0)
    second = jnp.sum(selected * pair_list[:, 1][:, None, None], axis=0)
    return first, second


def shards(traces, pair_list, pair_owner):
    win_local, chan_local, samples = traces.shape
    bin_count = samples // 2
    bands = lax.axis_size("band")
    owners = lax.axis_size("pair")
    band_bins = bin_count // bands
    per_device = chan_local // BLOCK
    per_slot = pair_list.shape[0] // (owners * SLOTS)

    flat = traces.reshape(win_local * chan_local, samples)
    halves = 2
    half_bins = band_bins // halves
    edges = [0, band_bins // 2, 3 * band_bins // 4, band_bins]
    spans = []
    for half in range(halves):
        ids = jnp.arange(bands * half_bins, dtype=jnp.int32)
        bins = (ids // half_bins) * band_bins + half * half_bins + ids % half_bins
        whitened = whiten(flat, bins)
        whitened = whitened.reshape(2, bands, half_bins, win_local, per_device, BLOCK)
        spans.append(jnp.transpose(whitened, (1, 4, 0, 3, 2, 5)))
    pieces = []
    for low, high in zip(edges[:-1], edges[1:]):
        parts = []
        for half in range(halves):
            start = max(low, half * half_bins)
            stop = min(high, (half + 1) * half_bins)
            if start < stop:
                parts.append(spans[half][:, :, :, :, start - half * half_bins:stop - half * half_bins, :])
        chunk_bins = parts[0] if len(parts) == 1 else jnp.concatenate(parts, axis=4)
        pieces.append(lax.all_to_all(chunk_bins, "band", split_axis=0, concat_axis=0, tiled=True))
    chunks = len(pieces)

    device_index = lax.axis_index("pair")
    slot_ids = device_index * SLOTS + jnp.arange(SLOTS, dtype=jnp.int32)
    first, second = slot_blocks(pair_list, pair_owner, slot_ids, per_slot)

    wanted = jnp.concatenate([first.reshape(-1), second.reshape(-1)])
    picks = (wanted[:, None] == jnp.arange(owners * per_device, dtype=jnp.int32)[None, :]).astype(jnp.bfloat16)
    products = []
    for part in range(chunks):
        piece = jnp.transpose(pieces[part], (1, 0, 2, 3, 4, 5))
        gathered = lax.all_gather(piece, "pair", axis=0, tiled=True)
        if part == chunks - 1 and part >= 1:
            gathered, products[-1] = lax.optimization_barrier((gathered, products[-1]))
        rows = gathered.shape[0]
        chosen = jnp.dot(picks, gathered.reshape(rows, -1), preferred_element_type=jnp.bfloat16)
        chosen = chosen.reshape(2, SLOTS, per_slot, *gathered.shape[1:])
        left = chosen[0]
        right = chosen[1]
        rotated = jnp.stack([-right[:, :, :, 1], right[:, :, :, 0]], axis=3)
        paired = jnp.stack([right, rotated], axis=1)
        product = jnp.einsum(
            "stgkwfa,sptgkwfb->spabf", left, paired, preferred_element_type=jnp.float32
        )
        product = product.astype(jnp.bfloat16)
        if part + 2 < chunks:
            pieces[part + 2], product = lax.optimization_barrier((pieces[part + 2], product))
        products.append(product)
    out = jnp.zeros((SLOTS, 2, BLOCK, BLOCK, band_bins), jnp.bfloat16)
    for part in range(chunks):
        out = lax.dynamic_update_slice_in_dim(out, products[part], edges[part], axis=4)
    return out


def solution(mesh):
    placed = (P("band", "pair", None), P(), P())
    return jax.shard_map(
        shards,
        mesh=mesh,
        in_specs=placed,
        out_specs=P("pair", None, None, None, "band"),
        check_vma=False,
    )
```

```python
import jax
import jax.numpy as jnp
from jax import lax
from jax.sharding import PartitionSpec as P

SUB = 64
BLOCK = 128
SLOTS = 2


whiten_eps = 1e-05


def dft_table(samples, bins):
    bin_ids = jnp.broadcast_to(bins[:, None], (bins.shape[0], samples))
    sample_ids = lax.broadcasted_iota(jnp.int32, (bins.shape[0], samples), 1)
    phase_angle = (sample_ids * bin_ids % samples).astype(jnp.float32) * (2.0 * jnp.pi / samples)
    return jnp.concatenate([jnp.cos(phase_angle), -jnp.sin(phase_angle)], axis=0)


def whiten(flat_traces, bins):
    row_count, samples = flat_traces.shape
    bin_count = bins.shape[0]
    spectra = lax.dot_general(
        dft_table(samples, bins),
        flat_traces,
        (((1,), (1,)), ((), ())),
        precision=lax.Precision.HIGH,
        preferred_element_type=jnp.float32,
    )
    real_band = spectra[:bin_count].reshape(bin_count // SUB, SUB, row_count)
    imag_band = spectra[bin_count:].reshape(bin_count // SUB, SUB, row_count)
    band_power = jnp.mean(real_band * real_band + imag_band * imag_band, axis=1, keepdims=True)
    factor = lax.rsqrt(band_power + whiten_eps)
    stacked = jnp.stack([real_band * factor, imag_band * factor], axis=0)
    return stacked.reshape(2, bin_count, row_count).astype(jnp.bfloat16)


def slot_blocks(pair_list, pair_owner, slot_ids, per_slot):
    slot_match = (pair_owner[:, None] == slot_ids[None, :]).astype(jnp.int32)
    slot_rank = jnp.cumsum(slot_match, axis=0) - 1
    rank_ids = jnp.arange(per_slot, dtype=jnp.int32)
    selected = slot_match[:, :, None] * (slot_rank[:, :, None] == rank_ids[None, None, :]).astype(jnp.int32)
    first = jnp.sum(selected * pair_list[:, 0][:, None, None], axis=0)
    second = jnp.sum(selected * pair_list[:, 1][:, None, None], axis=0)
    return first, second


def shards(traces, pair_list, pair_owner):
    win_local, chan_local, samples = traces.shape
    bin_count = samples // 2
    bands = lax.axis_size("band")
    owners = lax.axis_size("pair")
    band_bins = bin_count // bands
    per_device = chan_local // BLOCK
    per_slot = pair_list.shape[0] // (owners * SLOTS)

    flat = traces.reshape(win_local * chan_local, samples)
    halves = 2
    half_bins = band_bins // halves
    edges = [0, band_bins // 2, band_bins]
    spans = []
    for half in range(halves):
        ids = jnp.arange(bands * half_bins, dtype=jnp.int32)
        bins = (ids // half_bins) * band_bins + half * half_bins + ids % half_bins
        whitened = whiten(flat, bins)
        whitened = whitened.reshape(2, bands, half_bins, win_local, per_device, BLOCK)
        spans.append(jnp.transpose(whitened, (1, 4, 0, 3, 2, 5)))
    pieces = []
    for low, high in zip(edges[:-1], edges[1:]):
        parts = []
        for half in range(halves):
            start = max(low, half * half_bins)
            stop = min(high, (half + 1) * half_bins)
            if start < stop:
                parts.append(spans[half][:, :, :, :, start - half * half_bins:stop - half * half_bins, :])
        chunk_bins = parts[0] if len(parts) == 1 else jnp.concatenate(parts, axis=4)
        pieces.append(lax.all_to_all(chunk_bins, "band", split_axis=0, concat_axis=0, tiled=True))
    chunks = len(pieces)

    device_index = lax.axis_index("pair")
    slot_ids = device_index * SLOTS + jnp.arange(SLOTS, dtype=jnp.int32)
    first, second = slot_blocks(pair_list, pair_owner, slot_ids, per_slot)

    wanted = jnp.concatenate([first.reshape(-1), second.reshape(-1)])
    picks = (wanted[:, None] == jnp.arange(owners * per_device, dtype=jnp.int32)[None, :]).astype(jnp.bfloat16)
    products = []
    for part in range(chunks):
        piece = jnp.transpose(pieces[part], (1, 0, 2, 3, 4, 5))
        gathered = lax.all_gather(piece, "pair", axis=0, tiled=True)
        if part == chunks - 1 and part >= 1:
            gathered, products[-1] = lax.optimization_barrier((gathered, products[-1]))
        rows = gathered.shape[0]
        chosen = jnp.dot(picks, gathered.reshape(rows, -1), preferred_element_type=jnp.bfloat16)
        chosen = chosen.reshape(2, SLOTS, per_slot, *gathered.shape[1:])
        left = chosen[0]
        right = chosen[1]
        rotated = jnp.stack([-right[:, :, :, 1], right[:, :, :, 0]], axis=3)
        paired = jnp.stack([right, rotated], axis=1)
        product = jnp.einsum(
            "stgkwfa,sptgkwfb->spabf", left, paired, preferred_element_type=jnp.float32
        )
        product = product.astype(jnp.bfloat16)
        if part + 2 < chunks:
            pieces[part + 2], product = lax.optimization_barrier((pieces[part + 2], product))
        products.append(product)
    out = jnp.zeros((SLOTS, 2, BLOCK, BLOCK, band_bins), jnp.bfloat16)
    for part in range(chunks):
        out = lax.dynamic_update_slice_in_dim(out, products[part], edges[part], axis=4)
    return out


def solution(mesh):
    placed = (P("band", "pair", None), P(), P())
    return jax.shard_map(
        shards,
        mesh=mesh,
        in_specs=placed,
        out_specs=P("pair", None, None, None, "band"),
        check_vma=False,
    )
```

```python
import numpy as np
import jax
import jax.numpy as jnp
from jax import lax
from jax.sharding import PartitionSpec as P

SUB = 64
BLOCK = 128
SLOTS = 2


whiten_eps = 1e-05


def dft_table(samples, bins):
    phase_angle = (np.arange(samples)[None, :] * bins[:, None] % samples) * (2.0 * np.pi / samples)
    return jnp.asarray(np.concatenate([np.cos(phase_angle), -np.sin(phase_angle)], axis=0).astype(np.float32))


def whiten(flat_traces, bins):
    row_count, samples = flat_traces.shape
    bin_count = bins.shape[0]
    spectra = lax.dot_general(
        dft_table(samples, bins),
        flat_traces,
        (((1,), (1,)), ((), ())),
        precision=lax.Precision.HIGH,
        preferred_element_type=jnp.float32,
    )
    real_band = spectra[:bin_count].reshape(bin_count // SUB, SUB, row_count)
    imag_band = spectra[bin_count:].reshape(bin_count // SUB, SUB, row_count)
    band_power = jnp.mean(real_band * real_band + imag_band * imag_band, axis=1, keepdims=True)
    factor = lax.rsqrt(band_power + whiten_eps)
    stacked = jnp.stack([real_band * factor, imag_band * factor], axis=0)
    return stacked.reshape(2, bin_count, row_count).astype(jnp.bfloat16)


def slot_blocks(pair_list, pair_owner, slot_ids, per_slot):
    slot_match = (pair_owner[:, None] == slot_ids[None, :]).astype(jnp.int32)
    slot_rank = jnp.cumsum(slot_match, axis=0) - 1
    rank_ids = jnp.arange(per_slot, dtype=jnp.int32)
    selected = slot_match[:, :, None] * (slot_rank[:, :, None] == rank_ids[None, None, :]).astype(jnp.int32)
    first = jnp.sum(selected * pair_list[:, 0][:, None, None], axis=0)
    second = jnp.sum(selected * pair_list[:, 1][:, None, None], axis=0)
    return first, second


def shards(traces, pair_list, pair_owner):
    win_local, chan_local, samples = traces.shape
    bin_count = samples // 2
    bands = lax.axis_size("band")
    owners = lax.axis_size("pair")
    band_bins = bin_count // bands
    per_device = chan_local // BLOCK
    per_slot = pair_list.shape[0] // (owners * SLOTS)

    flat = traces.reshape(win_local * chan_local, samples)
    halves = 2
    half_bins = band_bins // halves
    edges = [0, band_bins // 2, 3 * band_bins // 4, band_bins]
    spans = []
    for half in range(halves):
        ids = np.arange(bands * half_bins)
        bins = (ids // half_bins) * band_bins + half * half_bins + ids % half_bins
        whitened = whiten(flat, bins)
        whitened = whitened.reshape(2, bands, half_bins, win_local, per_device, BLOCK)
        spans.append(jnp.transpose(whitened, (1, 4, 0, 3, 2, 5)))
    pieces = []
    for low, high in zip(edges[:-1], edges[1:]):
        parts = []
        for half in range(halves):
            start = max(low, half * half_bins)
            stop = min(high, (half + 1) * half_bins)
            if start < stop:
                parts.append(spans[half][:, :, :, :, start - half * half_bins:stop - half * half_bins, :])
        chunk_bins = parts[0] if len(parts) == 1 else jnp.concatenate(parts, axis=4)
        pieces.append(lax.all_to_all(chunk_bins, "band", split_axis=0, concat_axis=0, tiled=True))
    chunks = len(pieces)

    device_index = lax.axis_index("pair")
    slot_ids = device_index * SLOTS + jnp.arange(SLOTS, dtype=jnp.int32)
    first, second = slot_blocks(pair_list, pair_owner, slot_ids, per_slot)

    wanted = jnp.concatenate([first.reshape(-1), second.reshape(-1)])
    picks = (wanted[:, None] == jnp.arange(owners * per_device, dtype=jnp.int32)[None, :]).astype(jnp.bfloat16)
    products = []
    for part in range(chunks):
        piece = jnp.transpose(pieces[part], (1, 0, 2, 3, 4, 5))
        gathered = lax.all_gather(piece, "pair", axis=0, tiled=True)
        if part == chunks - 1 and part >= 1:
            gathered, products[-1] = lax.optimization_barrier((gathered, products[-1]))
        rows = gathered.shape[0]
        chosen = jnp.dot(picks, gathered.reshape(rows, -1), preferred_element_type=jnp.bfloat16)
        chosen = chosen.reshape(2, SLOTS, per_slot, *gathered.shape[1:])
        left = chosen[0]
        right = chosen[1]
        rotated = jnp.stack([-right[:, :, :, 1], right[:, :, :, 0]], axis=3)
        paired = jnp.stack([right, rotated], axis=1)
        product = jnp.einsum(
            "stgkwfa,sptgkwfb->spabf", left, paired, preferred_element_type=jnp.float32
        )
        product = product.astype(jnp.bfloat16)
        if part + 2 < chunks:
            pieces[part + 2], product = lax.optimization_barrier((pieces[part + 2], product))
        products.append(product)
    out = jnp.zeros((SLOTS, 2, BLOCK, BLOCK, band_bins), jnp.bfloat16)
    for part in range(chunks):
        out = lax.dynamic_update_slice_in_dim(out, products[part], edges[part], axis=4)
    return out


def solution(mesh):
    placed = (P("band", "pair", None), P(), P())
    return jax.shard_map(
        shards,
        mesh=mesh,
        in_specs=placed,
        out_specs=P("pair", None, None, None, "band"),
        check_vma=False,
    )
```
